256 devices in a mesh: ctx: 64 (over x_hi, z, y), mp: 4 (over x_lo, core).
Axes of the slice: x: 4 (x_hi: 2, x_lo: 2; x = x_hi * 2 + x_lo), y: 4, z: 8, core: 2. Of those that a mesh axis runs over, the one named last changes fastest.
Arguments:
- q_mr: bfloat16 [16384, 4096], P('ctx', 'mp'), may hold values from -6 to 6
- k_mr: bfloat16 [16384, 4096], P('ctx', 'mp'), may hold values from -6 to 6
- v_mr: bfloat16 [16384, 4096], P('ctx', 'mp'), may hold values from -6 to 6
- q_li: bfloat16 [16384, 4096], P('ctx', 'mp'), may hold values from -6 to 6
- k_li: bfloat16 [16384, 4096], P('ctx', 'mp'), may hold values from -6 to 6
- short_taps: float32 [6, 3, 4096], P(None, None, 'mp'), may hold values from -3.5 to 3.5
- mr_taps: float32 [128, 4096], P(None, 'mp'), may hold values from -0.5 to 0.5
- norm_gain: float32 [4096], P('mp'), may hold values from 0.1 to 1.9
- decay_rate: float32 [16, 4096], P(None, 'mp'), may hold values from 1.8310548e-05 to 0.03
- residue: float32 [16, 4096], P(None, 'mp'), may hold values from -1.5 to 1.5
Outputs:
- mixer_mr: bfloat16 [16384, 4096], P('ctx', 'mp')
- mixer_li: bfloat16 [16384, 4096], P('ctx', 'mp')
The draws below stay inside these ranges and needn't reach their ends.
All inputs are finite; a program needn't handle non-finite values.
Results may differ from the reference program's by a relative error of at most 0.0078.
Values may be sent and summed in bfloat16 or wider, within the bound.
No kernel may reach another device: no remote copies, remote signals or barrier semaphores. Data moves between devices by JAX's collectives and lax.ppermute only.
A program may use at most 64 MiB of HBM per device.

```python
import math
import jax
import jax.numpy as jnp
from jax import lax

D = 4096
FILT = 128
SHORT = 3
MODES = 16
SEQ = 16384


def levels(key, shape, split, low, high):
    def one(axis_at, parts):
        draws = jax.random.uniform(jax.random.fold_in(jax.random.fold_in(key, 6), axis_at), (parts,), jnp.float32, low / len(split), high / len(split))
        return jnp.repeat(jnp.exp(draws), shape[axis_at] // parts).reshape((-1,) + (1,) * (len(shape) - axis_at - 1))

    gain = one(*split[0])
    for cut in split[1:]:
        gain = gain * one(*cut)
    return gain


def normal_values(stream_key, dims, scale, most, shards=(), kind=jnp.bfloat16):
    values = jax.random.normal(stream_key, dims, jnp.float32) * scale
    if len(shards) > 0:
        values = levels(stream_key, dims, shards, -0.22, 0.18) * values
    return jnp.clip(values, min=-most, max=most).astype(kind)


def setup_inputs(seed: int = 0) -> dict:
    splits = jax.random.split(jax.random.key(seed), 11)
    q_mr = normal_values(splits[0], (SEQ, D), 1.0, 6.0, ((0, 64), (1, 4)))
    k_mr = normal_values(splits[1], (SEQ, D), 1.0, 6.0, ((0, 64), (1, 4)))
    v_mr = normal_values(splits[2], (SEQ, D), 1.0, 6.0, ((0, 64), (1, 4)))
    q_li = normal_values(splits[3], (SEQ, D), 1.0, 6.0, ((0, 64), (1, 4)))
    k_li = normal_values(splits[4], (SEQ, D), 1.0, 6.0, ((0, 64), (1, 4)))
    short_taps = normal_values(splits[5], (6, SHORT, D), SHORT ** -0.5, 3.5, ((2, 4),), jnp.float32)
    mr_taps = normal_values(splits[6], (FILT, D), FILT ** -0.5, 0.5, ((1, 4),), jnp.float32)
    norm_gain = jnp.clip(1.0 + 0.18 * jax.random.normal(splits[7], (D,), jnp.float32), 0.1, 1.9)
    decay_rate = jnp.clip(jnp.exp(math.log(0.03) - 7.4014754 * jax.random.uniform(splits[8], (MODES, D), jnp.float32) ** levels(splits[8], (MODES, D), ((1, 4),), -0.2, 0.2)), 1.831054760259576e-05, 0.03)
    residue = normal_values(splits[9], (MODES, D), 0.25, 1.5, ((1, 4),), jnp.float32)
    return {"q_mr": q_mr, "k_mr": k_mr, "v_mr": v_mr, "q_li": q_li, "k_li": k_li, "short_taps": short_taps, "mr_taps": mr_taps, "norm_gain": norm_gain, "decay_rate": decay_rate, "residue": residue}


def settle(values):
    return lax.optimization_barrier(values.astype(jnp.bfloat16))

def lag_conv(stream, taps):
    length = stream.shape[0]
    width = taps.shape[0]
    padded = jnp.pad(stream, ((width - 1, 0), (0, 0)))

    def add_lag(total, pair):
        lag, tap = pair
        start = (width - 1 - lag).astype(jnp.int32)
        piece = lax.dynamic_slice_in_dim(padded, start, length, 0)
        return (total + tap[None, :] * piece, None)
    lags = jnp.arange(width).astype(jnp.int32)
    total, _ = lax.scan(add_lag, jnp.zeros(stream.shape, jnp.float32).astype(stream.dtype), (lags, taps))
    return total

def short_conv(stream, taps):
    return lag_conv(stream.astype(jnp.float32), taps)

def mode_weight(rate, res):
    return res * jnp.sqrt(-jnp.expm1(-2.0 * rate))

def filter_table(rate, residue, length):
    times = jnp.arange(length).astype(jnp.float32)[:, None]

    def add_mode(total, pair):
        one_rate, one_res = pair
        return (total + mode_weight(one_rate, one_res)[None, :] * jnp.exp(-one_rate[None, :] * times), None)
    start = jnp.zeros((length, rate.shape[1]), jnp.float32)
    table, _ = lax.scan(add_mode, start, (rate, residue))
    return table

def block_ends(blocks, rate):
    length = blocks.shape[1]
    lags = (length - 1 - jnp.arange(length)).astype(jnp.float32)[:, None]

    def one_mode(carry, one_rate):
        return (carry, lax.optimization_barrier(jnp.sum(blocks * jnp.exp(-one_rate[None, :] * lags)[None], axis=1)))
    _, ends = lax.scan(one_mode, jnp.zeros((), jnp.float32), rate)
    return jnp.swapaxes(ends, 0, 1)

def carried_terms(starts, rate, residue, length):
    times = (jnp.arange(length) + 1).astype(jnp.float32)[:, None]

    def add_mode(total, triple):
        one_rate, one_res, state = triple
        factor = mode_weight(one_rate, one_res)[None, :] * jnp.exp(-one_rate[None, :] * times)
        return (total + factor[None] * state[:, None, :], None)
    start = jnp.zeros((starts.shape[0], length, rate.shape[1]), jnp.float32)
    total, _ = lax.scan(add_mode, start, (rate, residue, jnp.swapaxes(starts, 0, 1)))
    return total

def reference(q_mr, k_mr, v_mr, q_li, k_li, short_taps, mr_taps, norm_gain, decay_rate, residue):
    sq = short_conv(q_mr, short_taps[0])
    sk = short_conv(k_mr, short_taps[1])
    sv = short_conv(v_mr, short_taps[2])
    u_mr = settle(sk * sv)
    mr_long = lag_conv(u_mr.astype(jnp.float32), mr_taps)
    mixer_mr = (sq * mr_long).astype(jnp.bfloat16)
    wide = mixer_mr.astype(jnp.float32)
    mean_sq = lax.optimization_barrier(jnp.mean(wide * wide, axis=1, keepdims=True))
    normed = settle(wide * lax.rsqrt(mean_sq + 1e-06) * norm_gain[None, :])
    lq = short_conv(q_li, short_taps[3])
    lk = short_conv(k_li, short_taps[4])
    lv = short_conv(normed, short_taps[5])
    u_li = settle(lk * lv)
    ref_block = 32
    blocks = u_li.astype(jnp.float32).reshape(SEQ // ref_block, ref_block, D)
    table = filter_table(decay_rate, residue, ref_block)
    lag = (jnp.arange(ref_block)[:, None] - jnp.arange(ref_block)[None, :]).astype(jnp.int32)
    picked = jnp.take(table, jnp.clip(lag, 0, ref_block - 1), axis=0)
    toeplitz = jnp.where((lag >= 0)[:, :, None], picked, jnp.zeros_like(picked))
    decay = jnp.exp(-decay_rate * ref_block)

    def advance(state, block):
        single = block[None]
        local = jnp.einsum('ijc,jc->ic', toeplitz, block, precision=lax.Precision.HIGHEST)
        carried = carried_terms(state[None], decay_rate, residue, ref_block)[0]
        ends = block_ends(single, decay_rate)[0]
        return (decay * state + ends, local + carried)
    _, outputs = lax.scan(advance, jnp.zeros((MODES, D), jnp.float32), blocks)
    long_li = settle(outputs.reshape(SEQ, D))
    mixer_li = (lq * long_li.astype(jnp.float32)).astype(jnp.bfloat16)
    return (mixer_mr, mixer_li)
```

```python
import jax
import jax.numpy as jnp
from jax import lax
from jax.experimental import pallas as pl
from jax.experimental.pallas import tpu as pltpu
from jax.sharding import PartitionSpec as P

def shifted(shard, axis, by):
    devices = lax.axis_size(axis)
    pairs = [(i, i + by) for i in range(devices) if 0 <= i + by < devices]
    return lax.ppermute(shard, axis, pairs)


def to_bf16(values):
    return lax.reduce_precision(values, exponent_bits=8, mantissa_bits=7)


def short_conv(extended, taps, length):
    width = taps.shape[0]
    x = extended.astype(jnp.float32)
    total = taps[0][None, :] * x[width - 1 : width - 1 + length]
    for lag in range(1, width):
        start = width - 1 - lag
        total = total + taps[lag][None, :] * x[start : start + length]
    return total


def long_conv(extended, taps):
    kernel = taps[::-1][:, None, :]
    return lax.conv_general_dilated(
        extended[None],
        kernel,
        (1,),
        "VALID",
        dimension_numbers=("NWC", "WIO", "NWC"),
        feature_group_count=taps.shape[1],
        precision=lax.Precision.HIGHEST,
    )[0]


def mode_weight(rate, res):
    return res * jnp.sqrt(-jnp.expm1(-2.0 * rate))


def carry_in(ends, rate, width):
    devices = lax.axis_size("ctx")
    radix = 4
    state = shifted(ends, "ctx", 1)
    for j in range(2, radix + 1):
        if j < devices:
            state = state + jnp.exp(-width * (j - 1) * rate) * shifted(ends, "ctx", j)
    span = radix
    while span < devices:
        total = state
        for j in range(1, radix):
            if j * span < devices:
                total = total + jnp.exp(-width * (j * span) * rate) * shifted(state, "ctx", j * span)
        state = total
        span *= radix
    return state


LANES = 512


def _recur_body(u_ref, a_ref, w_ref, s0_ref, y_ref, end_ref):
    tokens, channels = u_ref.shape
    modes = a_ref.shape[0]
    for c0 in range(0, channels, LANES):
        cols = pl.ds(c0, LANES)
        a = a_ref[:, cols]
        w = w_ref[:, cols] if w_ref is not None else None

        def step(t, state):
            row = u_ref[pl.ds(t, 1), cols]
            state = a * state + row
            if y_ref is not None:
                y_ref[pl.ds(t, 1), cols] = jnp.sum(w * state, axis=0, keepdims=True)
            return state

        init = s0_ref[:, cols] if s0_ref is not None else jnp.zeros(a.shape, jnp.float32)
        state = lax.fori_loop(0, tokens, step, init, unroll=8)
        if end_ref is not None:
            end_ref[:, cols] = state


def _ends_kernel(u_ref, a_ref, end_ref):
    _recur_body(u_ref, a_ref, None, None, None, end_ref)


def _output_kernel(u_ref, a_ref, w_ref, s0_ref, y_ref):
    _recur_body(u_ref, a_ref, w_ref, s0_ref, y_ref, None)


def _vmem():
    return pl.BlockSpec(memory_space=pltpu.VMEM)


def recur_ends(u, a):
    tokens, channels = u.shape
    modes = a.shape[0]
    return pl.pallas_call(
        _ends_kernel,
        out_shape=jax.ShapeDtypeStruct(a.shape, jnp.float32),
        in_specs=[_vmem(), _vmem()],
        out_specs=_vmem(),
        cost_estimate=pl.CostEstimate(
            flops=2 * tokens * modes * channels, bytes_accessed=4 * (tokens + 2 * modes) * channels, transcendentals=0
        ),
    )(u, a)


def recur_output(u, a, w, s0):
    tokens, channels = u.shape
    modes = a.shape[0]
    return pl.pallas_call(
        _output_kernel,
        out_shape=jax.ShapeDtypeStruct(u.shape, jnp.float32),
        in_specs=[_vmem(), _vmem(), _vmem(), _vmem()],
        out_specs=_vmem(),
        cost_estimate=pl.CostEstimate(
            flops=4 * tokens * modes * channels, bytes_accessed=4 * (2 * tokens + 3 * modes) * channels, transcendentals=0
        ),
    )(u, a, w, s0)


def modal_long(u, rate, res):
    tokens = u.shape[0]
    weight = mode_weight(rate, res)
    a = jnp.exp(-rate)
    device_end = recur_ends(u, a)
    start_in = carry_in(device_end, rate, tokens)
    return recur_output(u, a, weight, start_in)


def shards(q_mr, k_mr, v_mr, q_li, k_li, short_taps, mr_taps, norm_gain, decay_rate, residue):
    tokens = q_mr.shape[0]
    width = short_taps.shape[1]
    short_rim = width - 1
    filt = mr_taps.shape[0]
    u_rows = filt - 1 + short_rim
    pack = 16
    sent_rows = -(-u_rows // pack) * pack
    tail = slice(tokens - sent_rows - short_rim, tokens)
    sk_tail = short_conv(k_mr[tail], short_taps[1], sent_rows)
    sv_tail = short_conv(v_mr[tail], short_taps[2], sent_rows)
    u_tail = (sk_tail * sv_tail).astype(jnp.bfloat16)
    q_rows = 2 * short_rim
    rims = [
        q_mr[tokens - q_rows :],
        k_mr[tokens - short_rim :],
        v_mr[tokens - short_rim :],
        q_li[tokens - short_rim :],
        k_li[tokens - short_rim :],
    ]
    small_rows = sum(r.shape[0] for r in rims)
    fill = jnp.zeros((-(-small_rows // pack) * pack - small_rows, q_mr.shape[1]), q_mr.dtype)
    got = shifted(jnp.concatenate([u_tail, jnp.concatenate(rims + [fill])]), "ctx", 1)
    u_rim = got[sent_rows - u_rows : sent_rows]
    at = sent_rows
    q_rim = got[at : at + q_rows]
    at += q_rows
    k_rim = got[at : at + short_rim]
    at += short_rim
    v_rim = got[at : at + short_rim]
    at += short_rim
    ql_rim = got[at : at + short_rim]
    at += short_rim
    kl_rim = got[at : at + short_rim]

    sk = short_conv(jnp.concatenate([k_rim, k_mr]), short_taps[1], tokens)
    sv = short_conv(jnp.concatenate([v_rim, v_mr]), short_taps[2], tokens)
    u_mr = (sk * sv).astype(jnp.bfloat16)
    u_ext = jnp.concatenate([u_rim, u_mr]).astype(jnp.float32)
    ext_rows = tokens + short_rim
    mr_long = long_conv(u_ext, mr_taps)
    sq = short_conv(jnp.concatenate([q_rim, q_mr]), short_taps[0], ext_rows)
    mixer_ext = to_bf16(sq * mr_long)
    mixer_mr = mixer_ext[short_rim:].astype(jnp.bfloat16)
    channels_all = mixer_ext.shape[1] * lax.axis_size("mp")
    totals = lax.psum(jnp.sum(mixer_ext * mixer_ext, axis=1), "mp")
    normed = to_bf16(mixer_ext * lax.rsqrt(totals / channels_all + 1e-06)[:, None] * norm_gain[None, :])
    lq = short_conv(jnp.concatenate([ql_rim, q_li]), short_taps[3], tokens)
    lk = short_conv(jnp.concatenate([kl_rim, k_li]), short_taps[4], tokens)
    lv = short_conv(normed, short_taps[5], tokens)
    u_li = to_bf16(lk * lv)
    long_li = to_bf16(modal_long(u_li, decay_rate, residue))
    mixer_li = (lq * long_li).astype(jnp.bfloat16)
    return (mixer_mr, mixer_li)


def solution(mesh):
    in_specs = (
        P("ctx", "mp"),
        P("ctx", "mp"),
        P("ctx", "mp"),
        P("ctx", "mp"),
        P("ctx", "mp"),
        P(None, None, "mp"),
        P(None, "mp"),
        P("mp"),
        P(None, "mp"),
        P(None, "mp"),
    )
    out_specs = (P("ctx", "mp"), P("ctx", "mp"))
    return jax.shard_map(shards, mesh=mesh, in_specs=in_specs, out_specs=out_specs, check_vma=False)
```

```python
import jax
import jax.numpy as jnp
from jax import lax
from jax.experimental import pallas as pl
from jax.experimental.pallas import tpu as pltpu
from jax.sharding import Mesh, PartitionSpec as P

CTX = ("xh", "z", "y")
LINK = jnp.float32


def ctx_size():
    return lax.axis_size("xh") * lax.axis_size("z") * lax.axis_size("y")


def shifted(shard, axis, by):
    devices = ctx_size() if axis == CTX else lax.axis_size(axis)
    pairs = [(i, i + by) for i in range(devices) if 0 <= i + by < devices]
    return lax.ppermute(shard, axis, pairs)


def to_bf16(values):
    return lax.reduce_precision(values, exponent_bits=8, mantissa_bits=7)


def short_conv(extended, taps, length):
    width = taps.shape[0]
    x = extended.astype(jnp.float32)
    total = taps[0][None, :] * x[width - 1 : width - 1 + length]
    for lag in range(1, width):
        start = width - 1 - lag
        total = total + taps[lag][None, :] * x[start : start + length]
    return total


def long_conv(extended, taps):
    kernel = taps[::-1][:, None, :]
    return lax.conv_general_dilated(
        extended[None],
        kernel,
        (1,),
        "VALID",
        dimension_numbers=("NWC", "WIO", "NWC"),
        feature_group_count=taps.shape[1],
        precision=lax.Precision.HIGHEST,
    )[0]


def mode_weight(rate, res):
    return res * jnp.sqrt(-jnp.expm1(-2.0 * rate))


def prefix(gathered, decay, me):
    before = jnp.zeros_like(gathered[0])
    total = jnp.zeros_like(gathered[0])
    for e in range(gathered.shape[0]):
        total = total * decay + gathered[e]
        before = jnp.where(e < me, total, before)
    return before, total


def carry_in(ends, rate, width):
    ny, nz = lax.axis_size("y"), lax.axis_size("z")
    y, z, x = lax.axis_index("y"), lax.axis_index("z"), lax.axis_index("xh")
    channels = ends.shape[1]
    quarter = channels // ny
    own = lax.dynamic_slice_in_dim(rate, y * quarter, quarter, 1)
    first = lax.all_gather(ends.astype(LINK), "y").astype(jnp.float32)
    in_group, group_end = prefix(first, jnp.exp(-width * rate), y)
    part = lax.dynamic_slice_in_dim(group_end, y * quarter, quarter, 1)
    second = lax.all_gather(part.astype(LINK), "z").astype(jnp.float32)
    in_half, half_end = prefix(second, jnp.exp(-width * ny * own), z)
    third = lax.all_gather(half_end.astype(LINK), "xh").astype(jnp.float32)
    in_whole, _ = prefix(third, jnp.exp(-width * ny * nz * own), x)
    group_start = in_half + jnp.exp(-width * ny * z.astype(jnp.float32) * own) * in_whole
    group_start = lax.all_gather(group_start.astype(LINK), "y", axis=1, tiled=True).astype(jnp.float32)
    return in_group + jnp.exp(-width * y.astype(jnp.float32) * rate) * group_start


LANES = 512


def _recur_body(u_ref, a_ref, w_ref, s0_ref, y_ref, end_ref):
    tokens, channels = u_ref.shape
    modes = a_ref.shape[0]
    for c0 in range(0, channels, LANES):
        cols = pl.ds(c0, LANES)
        a = a_ref[:, cols]
        w = w_ref[:, cols] if w_ref is not None else None

        def step(t, state):
            row = u_ref[pl.ds(t, 1), cols]
            state = a * state + row
            if y_ref is not None:
                y_ref[pl.ds(t, 1), cols] = jnp.sum(w * state, axis=0, keepdims=True)
            return state

        init = s0_ref[:, cols] if s0_ref is not None else jnp.zeros(a.shape, jnp.float32)
        state = lax.fori_loop(0, tokens, step, init, unroll=8)
        if end_ref is not None:
            end_ref[:, cols] = state


def _ends_kernel(u_ref, a_ref, end_ref):
    _recur_body(u_ref, a_ref, None, None, None, end_ref)


def _output_kernel(u_ref, a_ref, w_ref, s0_ref, y_ref):
    _recur_body(u_ref, a_ref, w_ref, s0_ref, y_ref, None)


def _vmem():
    return pl.BlockSpec(memory_space=pltpu.VMEM)


def recur_ends(u, a):
    tokens, channels = u.shape
    modes = a.shape[0]
    return pl.pallas_call(
        _ends_kernel,
        out_shape=jax.ShapeDtypeStruct(a.shape, jnp.float32),
        in_specs=[_vmem(), _vmem()],
        out_specs=_vmem(),
        cost_estimate=pl.CostEstimate(
            flops=2 * tokens * modes * channels, bytes_accessed=4 * (tokens + 2 * modes) * channels, transcendentals=0
        ),
    )(u, a)


def recur_output(u, a, w, s0):
    tokens, channels = u.shape
    modes = a.shape[0]
    return pl.pallas_call(
        _output_kernel,
        out_shape=jax.ShapeDtypeStruct(u.shape, jnp.float32),
        in_specs=[_vmem(), _vmem(), _vmem(), _vmem()],
        out_specs=_vmem(),
        cost_estimate=pl.CostEstimate(
            flops=4 * tokens * modes * channels, bytes_accessed=4 * (2 * tokens + 3 * modes) * channels, transcendentals=0
        ),
    )(u, a, w, s0)


def modal_long(u, rate, res):
    tokens = u.shape[0]
    weight = mode_weight(rate, res)
    a = jnp.exp(-rate)
    device_end = recur_ends(u, a)
    start_in = carry_in(device_end, rate, tokens)
    return recur_output(u, a, weight, start_in)


def shards(q_mr, k_mr, v_mr, q_li, k_li, short_taps, mr_taps, norm_gain, decay_rate, residue):
    tokens = q_mr.shape[0]
    width = short_taps.shape[1]
    short_rim = width - 1
    filt = mr_taps.shape[0]
    u_rows = filt - 1 + short_rim
    pack = 16
    sent_rows = -(-u_rows // pack) * pack
    tail = slice(tokens - sent_rows - short_rim, tokens)
    sk_tail = short_conv(k_mr[tail], short_taps[1], sent_rows)
    sv_tail = short_conv(v_mr[tail], short_taps[2], sent_rows)
    u_tail = (sk_tail * sv_tail).astype(jnp.bfloat16)
    q_rows = 2 * short_rim
    rims = [
        q_mr[tokens - q_rows :],
        k_mr[tokens - short_rim :],
        v_mr[tokens - short_rim :],
        q_li[tokens - short_rim :],
        k_li[tokens - short_rim :],
    ]
    small_rows = sum(r.shape[0] for r in rims)
    fill = jnp.zeros((-(-small_rows // pack) * pack - small_rows, q_mr.shape[1]), q_mr.dtype)
    got = shifted(jnp.concatenate([u_tail, jnp.concatenate(rims + [fill])]), CTX, 1)
    u_rim = got[sent_rows - u_rows : sent_rows]
    at = sent_rows
    q_rim = got[at : at + q_rows]
    at += q_rows
    k_rim = got[at : at + short_rim]
    at += short_rim
    v_rim = got[at : at + short_rim]
    at += short_rim
    ql_rim = got[at : at + short_rim]
    at += short_rim
    kl_rim = got[at : at + short_rim]

    sk = short_conv(jnp.concatenate([k_rim, k_mr]), short_taps[1], tokens)
    sv = short_conv(jnp.concatenate([v_rim, v_mr]), short_taps[2], tokens)
    u_mr = (sk * sv).astype(jnp.bfloat16)
    u_ext = jnp.concatenate([u_rim, u_mr]).astype(jnp.float32)
    ext_rows = tokens + short_rim
    mr_long = long_conv(u_ext, mr_taps)
    sq = short_conv(jnp.concatenate([q_rim, q_mr]), short_taps[0], ext_rows)
    mixer_ext = to_bf16(sq * mr_long)
    mixer_mr = mixer_ext[short_rim:].astype(jnp.bfloat16)
    channels_all = mixer_ext.shape[1] * lax.axis_size("mp")
    totals = lax.psum(jnp.sum(mixer_ext * mixer_ext, axis=1), "mp")
    normed = to_bf16(mixer_ext * lax.rsqrt(totals / channels_all + 1e-06)[:, None] * norm_gain[None, :])
    lq = short_conv(jnp.concatenate([ql_rim, q_li]), short_taps[3], tokens)
    lk = short_conv(jnp.concatenate([kl_rim, k_li]), short_taps[4], tokens)
    lv = short_conv(normed, short_taps[5], tokens)
    u_li = to_bf16(lk * lv)
    long_li = to_bf16(modal_long(u_li, decay_rate, residue))
    mixer_li = (lq * long_li).astype(jnp.bfloat16)
    return (mixer_mr, mixer_li)


def solution(mesh):
    ctx, mp = mesh.shape["ctx"], mesh.shape["mp"]
    ny = 4
    nz = 8
    nx = ctx // (ny * nz)
    grid = Mesh(mesh.devices.reshape(nx, nz, ny, mp), ("xh", "z", "y", "mp"))
    in_specs = (
        P(CTX, "mp"),
        P(CTX, "mp"),
        P(CTX, "mp"),
        P(CTX, "mp"),
        P(CTX, "mp"),
        P(None, None, "mp"),
        P(None, "mp"),
        P("mp"),
        P(None, "mp"),
        P(None, "mp"),
    )
    out_specs = (P(CTX, "mp"), P(CTX, "mp"))
    return jax.shard_map(shards, mesh=grid, in_specs=in_specs, out_specs=out_specs, check_vma=False)
```

```python
import jax
import jax.numpy as jnp
from jax import lax
from jax.experimental import pallas as pl
from jax.experimental.pallas import tpu as pltpu
from jax.sharding import PartitionSpec as P

def shifted(shard, axis, by):
    devices = lax.axis_size(axis)
    pairs = [(i, i + by) for i in range(devices) if 0 <= i + by < devices]
    return lax.ppermute(shard, axis, pairs)


def to_bf16(values):
    return lax.reduce_precision(values, exponent_bits=8, mantissa_bits=7)


def short_conv(extended, taps, length):
    width = taps.shape[0]
    x = extended.astype(jnp.float32)
    total = taps[0][None, :] * x[width - 1 : width - 1 + length]
    for lag in range(1, width):
        start = width - 1 - lag
        total = total + taps[lag][None, :] * x[start : start + length]
    return total


def long_conv(extended, taps):
    kernel = taps[::-1][:, None, :]
    return lax.conv_general_dilated(
        extended[None],
        kernel,
        (1,),
        "VALID",
        dimension_numbers=("NWC", "WIO", "NWC"),
        feature_group_count=taps.shape[1],
        precision=lax.Precision.HIGHEST,
    )[0]


def mode_weight(rate, res):
    return res * jnp.sqrt(-jnp.expm1(-2.0 * rate))


def carry_in(ends, rate, width):
    devices = lax.axis_size("ctx")
    radix = 4
    sent = ends.astype(jnp.bfloat16)
    state = shifted(sent, "ctx", 1).astype(jnp.float32)
    for j in range(2, radix + 1):
        if j < devices:
            state = state + jnp.exp(-width * (j - 1) * rate) * shifted(sent, "ctx", j).astype(jnp.float32)
    span = radix
    while span < devices:
        total = state
        sent = state.astype(jnp.bfloat16)
        for j in range(1, radix):
            if j * span < devices:
                got = shifted(sent, "ctx", j * span).astype(jnp.float32)
                total = total + jnp.exp(-width * (j * span) * rate) * got
        state = total
        span *= radix
    return state


LANES = 512


def _recur_body(u_ref, a_ref, w_ref, s0_ref, y_ref, end_ref):
    tokens, channels = u_ref.shape
    modes = a_ref.shape[0]
    for c0 in range(0, channels, LANES):
        cols = pl.ds(c0, LANES)
        a = a_ref[:, cols]
        w = w_ref[:, cols] if w_ref is not None else None

        def step(t, state):
            row = u_ref[pl.ds(t, 1), cols]
            state = a * state + row
            if y_ref is not None:
                y_ref[pl.ds(t, 1), cols] = jnp.sum(w * state, axis=0, keepdims=True)
            return state

        init = s0_ref[:, cols] if s0_ref is not None else jnp.zeros(a.shape, jnp.float32)
        state = lax.fori_loop(0, tokens, step, init, unroll=8)
        if end_ref is not None:
            end_ref[:, cols] = state


def _ends_kernel(u_ref, a_ref, end_ref):
    _recur_body(u_ref, a_ref, None, None, None, end_ref)


def _output_kernel(u_ref, a_ref, w_ref, s0_ref, y_ref):
    _recur_body(u_ref, a_ref, w_ref, s0_ref, y_ref, None)


def _vmem():
    return pl.BlockSpec(memory_space=pltpu.VMEM)


def recur_ends(u, a):
    tokens, channels = u.shape
    modes = a.shape[0]
    return pl.pallas_call(
        _ends_kernel,
        out_shape=jax.ShapeDtypeStruct(a.shape, jnp.float32),
        in_specs=[_vmem(), _vmem()],
        out_specs=_vmem(),
        cost_estimate=pl.CostEstimate(
            flops=2 * tokens * modes * channels, bytes_accessed=4 * (tokens + 2 * modes) * channels, transcendentals=0
        ),
    )(u, a)


def recur_output(u, a, w, s0):
    tokens, channels = u.shape
    modes = a.shape[0]
    return pl.pallas_call(
        _output_kernel,
        out_shape=jax.ShapeDtypeStruct(u.shape, jnp.float32),
        in_specs=[_vmem(), _vmem(), _vmem(), _vmem()],
        out_specs=_vmem(),
        cost_estimate=pl.CostEstimate(
            flops=4 * tokens * modes * channels, bytes_accessed=4 * (2 * tokens + 3 * modes) * channels, transcendentals=0
        ),
    )(u, a, w, s0)


def modal_long(u, rate, res):
    tokens = u.shape[0]
    weight = mode_weight(rate, res)
    a = jnp.exp(-rate)
    device_end = recur_ends(u, a)
    start_in = carry_in(device_end, rate, tokens)
    return recur_output(u, a, weight, start_in)


def shards(q_mr, k_mr, v_mr, q_li, k_li, short_taps, mr_taps, norm_gain, decay_rate, residue):
    tokens = q_mr.shape[0]
    width = short_taps.shape[1]
    short_rim = width - 1
    filt = mr_taps.shape[0]
    u_rows = filt - 1 + short_rim
    pack = 16
    sent_rows = -(-u_rows // pack) * pack
    tail = slice(tokens - sent_rows - short_rim, tokens)
    sk_tail = short_conv(k_mr[tail], short_taps[1], sent_rows)
    sv_tail = short_conv(v_mr[tail], short_taps[2], sent_rows)
    u_tail = (sk_tail * sv_tail).astype(jnp.bfloat16)
    q_rows = 2 * short_rim
    rims = [
        q_mr[tokens - q_rows :],
        k_mr[tokens - short_rim :],
        v_mr[tokens - short_rim :],
        q_li[tokens - short_rim :],
        k_li[tokens - short_rim :],
    ]
    small_rows = sum(r.shape[0] for r in rims)
    fill = jnp.zeros((-(-small_rows // pack) * pack - small_rows, q_mr.shape[1]), q_mr.dtype)
    got = shifted(jnp.concatenate([u_tail, jnp.concatenate(rims + [fill])]), "ctx", 1)
    u_rim = got[sent_rows - u_rows : sent_rows]
    at = sent_rows
    q_rim = got[at : at + q_rows]
    at += q_rows
    k_rim = got[at : at + short_rim]
    at += short_rim
    v_rim = got[at : at + short_rim]
    at += short_rim
    ql_rim = got[at : at + short_rim]
    at += short_rim
    kl_rim = got[at : at + short_rim]

    sk = short_conv(jnp.concatenate([k_rim, k_mr]), short_taps[1], tokens)
    sv = short_conv(jnp.concatenate([v_rim, v_mr]), short_taps[2], tokens)
    u_mr = (sk * sv).astype(jnp.bfloat16)
    u_ext = jnp.concatenate([u_rim, u_mr]).astype(jnp.float32)
    ext_rows = tokens + short_rim
    mr_long = long_conv(u_ext, mr_taps)
    sq = short_conv(jnp.concatenate([q_rim, q_mr]), short_taps[0], ext_rows)
    mixer_ext = to_bf16(sq * mr_long)
    mixer_mr = mixer_ext[short_rim:].astype(jnp.bfloat16)
    channels_all = mixer_ext.shape[1] * lax.axis_size("mp")
    totals = lax.psum(jnp.sum(mixer_ext * mixer_ext, axis=1), "mp")
    normed = to_bf16(mixer_ext * lax.rsqrt(totals / channels_all + 1e-06)[:, None] * norm_gain[None, :])
    lq = short_conv(jnp.concatenate([ql_rim, q_li]), short_taps[3], tokens)
    lk = short_conv(jnp.concatenate([kl_rim, k_li]), short_taps[4], tokens)
    lv = short_conv(normed, short_taps[5], tokens)
    u_li = to_bf16(lk * lv)
    long_li = to_bf16(modal_long(u_li, decay_rate, residue))
    mixer_li = (lq * long_li).astype(jnp.bfloat16)
    return (mixer_mr, mixer_li)


def solution(mesh):
    in_specs = (
        P("ctx", "mp"),
        P("ctx", "mp"),
        P("ctx", "mp"),
        P("ctx", "mp"),
        P("ctx", "mp"),
        P(None, None, "mp"),
        P(None, "mp"),
        P("mp"),
        P(None, "mp"),
        P(None, "mp"),
    )
    out_specs = (P("ctx", "mp"), P("ctx", "mp"))
    return jax.shard_map(shards, mesh=mesh, in_specs=in_specs, out_specs=out_specs, check_vma=False)
```

```python
import jax
import jax.numpy as jnp
from jax import lax
from jax.experimental import pallas as pl
from jax.experimental.pallas import tpu as pltpu
from jax.sharding import PartitionSpec as P

def shifted(shard, axis, by):
    devices = lax.axis_size(axis)
    pairs = [(i, i + by) for i in range(devices) if 0 <= i + by < devices]
    return lax.ppermute(shard, axis, pairs)


def to_bf16(values):
    return lax.reduce_precision(values, exponent_bits=8, mantissa_bits=7)


def short_conv(extended, taps, length):
    width = taps.shape[0]
    x = extended.astype(jnp.float32)
    total = taps[0][None, :] * x[width - 1 : width - 1 + length]
    for lag in range(1, width):
        start = width - 1 - lag
        total = total + taps[lag][None, :] * x[start : start + length]
    return total


def long_conv(extended, taps):
    kernel = taps[::-1][:, None, :]
    return lax.conv_general_dilated(
        extended[None],
        kernel,
        (1,),
        "VALID",
        dimension_numbers=("NWC", "WIO", "NWC"),
        feature_group_count=taps.shape[1],
        precision=lax.Precision.HIGHEST,
    )[0]


def mode_weight(rate, res):
    return res * jnp.sqrt(-jnp.expm1(-2.0 * rate))


def carry_in(ends, rate, width):
    devices = lax.axis_size("ctx")
    radix = 4
    sent = ends.astype(jnp.bfloat16)
    state = shifted(sent, "ctx", 1).astype(jnp.float32)
    for j in range(2, radix + 1):
        if j < devices:
            state = state + jnp.exp(-width * (j - 1) * rate) * shifted(sent, "ctx", j).astype(jnp.float32)
    span = radix
    while span < devices:
        total = state
        sent = state.astype(jnp.bfloat16)
        for j in range(1, radix):
            if j * span < devices:
                got = shifted(sent, "ctx", j * span).astype(jnp.float32)
                total = total + jnp.exp(-width * (j * span) * rate) * got
        state = total
        span *= radix
    return state


LANES = 1024


def _recur_body(u_ref, a_ref, w_ref, s0_ref, y_ref, end_ref):
    tokens, channels = u_ref.shape
    modes = a_ref.shape[0]
    for c0 in range(0, channels, LANES):
        cols = pl.ds(c0, LANES)
        a = a_ref[:, cols]
        w = w_ref[:, cols] if w_ref is not None else None

        def step(t, state):
            row = u_ref[pl.ds(t, 1), cols]
            state = a * state + row
            if y_ref is not None:
                y_ref[pl.ds(t, 1), cols] = jnp.sum(w * state, axis=0, keepdims=True)
            return state

        init = s0_ref[:, cols] if s0_ref is not None else jnp.zeros(a.shape, jnp.float32)
        state = lax.fori_loop(0, tokens, step, init, unroll=8)
        if end_ref is not None:
            end_ref[:, cols] = state


def _ends_kernel(u_ref, a_ref, end_ref):
    _recur_body(u_ref, a_ref, None, None, None, end_ref)


def _output_kernel(u_ref, a_ref, w_ref, s0_ref, y_ref):
    _recur_body(u_ref, a_ref, w_ref, s0_ref, y_ref, None)


def _vmem():
    return pl.BlockSpec(memory_space=pltpu.VMEM)


def recur_ends(u, a):
    tokens, channels = u.shape
    modes = a.shape[0]
    return pl.pallas_call(
        _ends_kernel,
        out_shape=jax.ShapeDtypeStruct(a.shape, jnp.float32),
        in_specs=[_vmem(), _vmem()],
        out_specs=_vmem(),
        cost_estimate=pl.CostEstimate(
            flops=2 * tokens * modes * channels, bytes_accessed=4 * (tokens + 2 * modes) * channels, transcendentals=0
        ),
    )(u, a)


def recur_output(u, a, w, s0):
    tokens, channels = u.shape
    modes = a.shape[0]
    return pl.pallas_call(
        _output_kernel,
        out_shape=jax.ShapeDtypeStruct(u.shape, jnp.float32),
        in_specs=[_vmem(), _vmem(), _vmem(), _vmem()],
        out_specs=_vmem(),
        cost_estimate=pl.CostEstimate(
            flops=4 * tokens * modes * channels, bytes_accessed=4 * (2 * tokens + 3 * modes) * channels, transcendentals=0
        ),
    )(u, a, w, s0)


def modal_long(u, rate, res):
    tokens = u.shape[0]
    weight = mode_weight(rate, res)
    a = jnp.exp(-rate)
    device_end = recur_ends(u, a)
    start_in = carry_in(device_end, rate, tokens)
    return recur_output(u, a, weight, start_in)


def shards(q_mr, k_mr, v_mr, q_li, k_li, short_taps, mr_taps, norm_gain, decay_rate, residue):
    tokens = q_mr.shape[0]
    width = short_taps.shape[1]
    short_rim = width - 1
    filt = mr_taps.shape[0]
    u_rows = filt - 1 + short_rim
    pack = 16
    sent_rows = -(-u_rows // pack) * pack
    tail = slice(tokens - sent_rows - short_rim, tokens)
    sk_tail = short_conv(k_mr[tail], short_taps[1], sent_rows)
    sv_tail = short_conv(v_mr[tail], short_taps[2], sent_rows)
    u_tail = (sk_tail * sv_tail).astype(jnp.bfloat16)
    q_rows = 2 * short_rim
    rims = [
        q_mr[tokens - q_rows :],
        k_mr[tokens - short_rim :],
        v_mr[tokens - short_rim :],
        q_li[tokens - short_rim :],
        k_li[tokens - short_rim :],
    ]
    small_rows = sum(r.shape[0] for r in rims)
    fill = jnp.zeros((-(-small_rows // pack) * pack - small_rows, q_mr.shape[1]), q_mr.dtype)
    got = shifted(jnp.concatenate([u_tail, jnp.concatenate(rims + [fill])]), "ctx", 1)
    u_rim = got[sent_rows - u_rows : sent_rows]
    at = sent_rows
    q_rim = got[at : at + q_rows]
    at += q_rows
    k_rim = got[at : at + short_rim]
    at += short_rim
    v_rim = got[at : at + short_rim]
    at += short_rim
    ql_rim = got[at : at + short_rim]
    at += short_rim
    kl_rim = got[at : at + short_rim]

    sk = short_conv(jnp.concatenate([k_rim, k_mr]), short_taps[1], tokens)
    sv = short_conv(jnp.concatenate([v_rim, v_mr]), short_taps[2], tokens)
    u_mr = (sk * sv).astype(jnp.bfloat16)
    u_ext = jnp.concatenate([u_rim, u_mr]).astype(jnp.float32)
    ext_rows = tokens + short_rim
    mr_long = long_conv(u_ext, mr_taps)
    sq = short_conv(jnp.concatenate([q_rim, q_mr]), short_taps[0], ext_rows)
    mixer_ext = to_bf16(sq * mr_long)
    mixer_mr = mixer_ext[short_rim:].astype(jnp.bfloat16)
    channels_all = mixer_ext.shape[1] * lax.axis_size("mp")
    totals = lax.psum(jnp.sum(mixer_ext * mixer_ext, axis=1), "mp")
    normed = to_bf16(mixer_ext * lax.rsqrt(totals / channels_all + 1e-06)[:, None] * norm_gain[None, :])
    lq = short_conv(jnp.concatenate([ql_rim, q_li]), short_taps[3], tokens)
    lk = short_conv(jnp.concatenate([kl_rim, k_li]), short_taps[4], tokens)
    lv = short_conv(normed, short_taps[5], tokens)
    u_li = to_bf16(lk * lv)
    long_li = to_bf16(modal_long(u_li, decay_rate, residue))
    mixer_li = (lq * long_li).astype(jnp.bfloat16)
    return (mixer_mr, mixer_li)


def solution(mesh):
    in_specs = (
        P("ctx", "mp"),
        P("ctx", "mp"),
        P("ctx", "mp"),
        P("ctx", "mp"),
        P("ctx", "mp"),
        P(None, None, "mp"),
        P(None, "mp"),
        P("mp"),
        P(None, "mp"),
        P(None, "mp"),
    )
    out_specs = (P("ctx", "mp"), P("ctx", "mp"))
    return jax.shard_map(shards, mesh=mesh, in_specs=in_specs, out_specs=out_specs, check_vma=False)
```

```python
import jax
import jax.numpy as jnp
from jax import lax
from jax.experimental import pallas as pl
from jax.experimental.pallas import tpu as pltpu
from jax.sharding import PartitionSpec as P

def shifted(shard, axis, by):
    devices = lax.axis_size(axis)
    pairs = [(i, i + by) for i in range(devices) if 0 <= i + by < devices]
    return lax.ppermute(shard, axis, pairs)


def to_bf16(values):
    return lax.reduce_precision(values, exponent_bits=8, mantissa_bits=7)


def short_conv(extended, taps, length):
    width = taps.shape[0]
    x = extended.astype(jnp.float32)
    total = taps[0][None, :] * x[width - 1 : width - 1 + length]
    for lag in range(1, width):
        start = width - 1 - lag
        total = total + taps[lag][None, :] * x[start : start + length]
    return total


def long_conv(extended, taps):
    kernel = taps[::-1][:, None, :]
    return lax.conv_general_dilated(
        extended[None],
        kernel,
        (1,),
        "VALID",
        dimension_numbers=("NWC", "WIO", "NWC"),
        feature_group_count=taps.shape[1],
        precision=lax.Precision.HIGHEST,
    )[0]


def mode_weight(rate, res):
    return res * jnp.sqrt(-jnp.expm1(-2.0 * rate))


def carry_in(ends, rate, width):
    devices = lax.axis_size("ctx")
    radix = 4
    sent = ends.astype(jnp.bfloat16)
    state = shifted(sent, "ctx", 1).astype(jnp.float32)
    for j in range(2, radix + 1):
        if j < devices:
            state = state + jnp.exp(-width * (j - 1) * rate) * shifted(sent, "ctx", j).astype(jnp.float32)
    span = radix
    while span < devices:
        total = state
        sent = state.astype(jnp.bfloat16)
        for j in range(1, radix):
            if j * span < devices:
                got = shifted(sent, "ctx", j * span).astype(jnp.float32)
                total = total + jnp.exp(-width * (j * span) * rate) * got
        state = total
        span *= radix
    return state


LANES = 512


def _recur_body(u_ref, a_ref, w_ref, s0_ref, y_ref, end_ref):
    tokens, channels = u_ref.shape
    modes = a_ref.shape[0]
    for c0 in range(0, channels, LANES):
        cols = pl.ds(c0, LANES)
        a = a_ref[:, cols]
        w = w_ref[:, cols] if w_ref is not None else None

        def step(t, state):
            row = u_ref[pl.ds(t, 1), cols]
            state = a * state + row
            if y_ref is not None:
                y_ref[pl.ds(t, 1), cols] = jnp.sum(w * state, axis=0, keepdims=True)
            return state

        init = s0_ref[:, cols] if s0_ref is not None else jnp.zeros(a.shape, jnp.float32)
        state = lax.fori_loop(0, tokens, step, init, unroll=8)
        if end_ref is not None:
            end_ref[:, cols] = state


def _ends_kernel(u_ref, a_ref, end_ref):
    _recur_body(u_ref, a_ref, None, None, None, end_ref)


def _output_kernel(u_ref, a_ref, w_ref, s0_ref, y_ref):
    _recur_body(u_ref, a_ref, w_ref, s0_ref, y_ref, None)


def _vmem():
    return pl.BlockSpec(memory_space=pltpu.VMEM)


def recur_ends(u, a):
    tokens, channels = u.shape
    modes = a.shape[0]
    return pl.pallas_call(
        _ends_kernel,
        out_shape=jax.ShapeDtypeStruct(a.shape, jnp.float32),
        in_specs=[_vmem(), _vmem()],
        out_specs=_vmem(),
        cost_estimate=pl.CostEstimate(
            flops=2 * tokens * modes * channels, bytes_accessed=4 * (tokens + 2 * modes) * channels, transcendentals=0
        ),
    )(u, a)


def recur_output(u, a, w, s0):
    tokens, channels = u.shape
    modes = a.shape[0]
    return pl.pallas_call(
        _output_kernel,
        out_shape=jax.ShapeDtypeStruct(u.shape, jnp.float32),
        in_specs=[_vmem(), _vmem(), _vmem(), _vmem()],
        out_specs=_vmem(),
        cost_estimate=pl.CostEstimate(
            flops=4 * tokens * modes * channels, bytes_accessed=4 * (2 * tokens + 3 * modes) * channels, transcendentals=0
        ),
    )(u, a, w, s0)


def modal_long(u, rate, res):
    tokens = u.shape[0]
    weight = mode_weight(rate, res)
    a = jnp.exp(-rate)
    device_end = recur_ends(u, a)
    start_in = carry_in(device_end, rate, tokens)
    return recur_output(u, a, weight, start_in)


def shards(q_mr, k_mr, v_mr, q_li, k_li, short_taps, mr_taps, norm_gain, decay_rate, residue):
    tokens = q_mr.shape[0]
    width = short_taps.shape[1]
    short_rim = width - 1
    filt = mr_taps.shape[0]
    u_rows = filt - 1 + short_rim
    pack = 16
    sent_rows = -(-u_rows // pack) * pack
    inner = tokens - short_rim
    u_loc = (short_conv(k_mr, short_taps[1], inner) * short_conv(v_mr, short_taps[2], inner)).astype(jnp.bfloat16)
    u_tail = u_loc[inner - sent_rows :]
    q_rows = 2 * short_rim
    rims = [
        q_mr[tokens - q_rows :],
        k_mr[tokens - short_rim :],
        v_mr[tokens - short_rim :],
        q_li[tokens - short_rim :],
        k_li[tokens - short_rim :],
    ]
    small_rows = sum(r.shape[0] for r in rims)
    fill = jnp.zeros((-(-small_rows // pack) * pack - small_rows, q_mr.shape[1]), q_mr.dtype)
    got = shifted(jnp.concatenate([u_tail, jnp.concatenate(rims + [fill])]), "ctx", 1)
    u_rim = got[sent_rows - u_rows : sent_rows]
    at = sent_rows
    q_rim = got[at : at + q_rows]
    at += q_rows
    k_rim = got[at : at + short_rim]
    at += short_rim
    v_rim = got[at : at + short_rim]
    at += short_rim
    ql_rim = got[at : at + short_rim]
    at += short_rim
    kl_rim = got[at : at + short_rim]

    sk = short_conv(jnp.concatenate([k_rim, k_mr[:short_rim]]), short_taps[1], short_rim)
    sv = short_conv(jnp.concatenate([v_rim, v_mr[:short_rim]]), short_taps[2], short_rim)
    u_head = (sk * sv).astype(jnp.bfloat16)
    ext_rows = tokens + short_rim
    local_rows = inner - (filt - 1)
    head = ext_rows - local_rows
    u_ext = jnp.concatenate([u_rim, u_head, u_loc[: head + filt - 1 - u_rows - short_rim]]).astype(jnp.float32)
    mr_long = jnp.concatenate([long_conv(u_ext, mr_taps), long_conv(u_loc.astype(jnp.float32), mr_taps)])
    sq = short_conv(jnp.concatenate([q_rim, q_mr]), short_taps[0], ext_rows)
    mixer_ext = to_bf16(sq * mr_long)
    mixer_mr = mixer_ext[short_rim:].astype(jnp.bfloat16)
    channels_all = mixer_ext.shape[1] * lax.axis_size("mp")
    totals = lax.psum(jnp.sum(mixer_ext * mixer_ext, axis=1), "mp")
    normed = to_bf16(mixer_ext * lax.rsqrt(totals / channels_all + 1e-06)[:, None] * norm_gain[None, :])
    lq = short_conv(jnp.concatenate([ql_rim, q_li]), short_taps[3], tokens)
    lk = short_conv(jnp.concatenate([kl_rim, k_li]), short_taps[4], tokens)
    lv = short_conv(normed, short_taps[5], tokens)
    u_li = to_bf16(lk * lv)
    long_li = to_bf16(modal_long(u_li, decay_rate, residue))
    mixer_li = (lq * long_li).astype(jnp.bfloat16)
    return (mixer_mr, mixer_li)


def solution(mesh):
    in_specs = (
        P("ctx", "mp"),
        P("ctx", "mp"),
        P("ctx", "mp"),
        P("ctx", "mp"),
        P("ctx", "mp"),
        P(None, None, "mp"),
        P(None, "mp"),
        P("mp"),
        P(None, "mp"),
        P(None, "mp"),
    )
    out_specs = (P("ctx", "mp"), P("ctx", "mp"))
    return jax.shard_map(shards, mesh=mesh, in_specs=in_specs, out_specs=out_specs, check_vma=False)
```
